256 devices in a mesh: gx: 64 (over z, y, core), gy: 4 (over x).
Axes of the slice: x: 4, y: 4, z: 8, core: 2. Of those that a mesh axis runs over, the one named last changes fastest.
Arguments:
- embeds: bfloat16 [256, 2048, 768], P('gx', 'gy'), may hold values from -6 to 6
- fetch_list: int32 [2, 64, 64], replicated, may hold values from 0 to 16383, as said below
- partners: int32 [2, 64, 64, 2], replicated, may hold values from 0 to 255, as said below
- counts: int32 [256], replicated, may hold values from 512 to 2048
Outputs:
- nearest: float32 [256, 2048], P('gx', 'gy')
The draws below stay inside these ranges and needn't reach their ends.
Inputs may be any that keep to these rules, and one draw needn't show every extreme that they name: fetch_list[w, h, g] // 64 is a block stored by index g of gx, that is g * 4 <= fetch_list[w, h, g] // 64 < (g + 1) * 4. partners[w, h, g, :] are 2 different blocks stored by index h of gx, none equal to fetch_list[w, h, g] // 64.
All inputs are finite; a program needn't handle non-finite values.
Results may differ from the reference program's by a relative error of at most 0.0003.
Values may be sent and summed in bfloat16 or wider, within the bound.
No kernel may reach another device: no remote copies, remote signals or barrier semaphores. Data moves between devices by JAX's collectives and lax.ppermute only.
A program may use at most 192 MiB of HBM per device.

```python
import jax
import jax.numpy as jnp
from jax import lax

D = 768
BLOCK = 2048
OWNED = 4
SLICE = 8
PARTNERS = 2
WAVES = 2
BLOCKS = 256
QUARTER = 512
PIECES = 64
N_GY = 4


def lender_local(key):
    groups = BLOCKS // OWNED
    return jax.random.randint(jax.random.fold_in(key, 11), (WAVES, groups, groups), 0, OWNED)


def draw_fetch_list(key, part):
    groups = BLOCKS // OWNED
    local = lender_local(key)
    piece = jax.random.randint(jax.random.fold_in(key, 37), (WAVES, groups, groups), 0, PIECES)
    owner = jnp.arange(groups, dtype=jnp.int32)[None, None, :] * OWNED
    return ((local + owner) * PIECES + piece).astype(jnp.int32)


def draw_partners(key, part):
    groups = BLOCKS // OWNED
    local = lender_local(key)
    raw = jax.random.randint(jax.random.fold_in(key, 23), (WAVES, groups, groups, OWNED - 1), 0, 1 << 20)
    scores = raw * (OWNED - 1) + jnp.arange(OWNED - 1, dtype=jnp.int32)
    offsets = jnp.argsort(scores, axis=-1)[..., :PARTNERS].astype(jnp.int32) + 1
    chosen = (local[..., None] + offsets) % OWNED
    worker = jnp.arange(groups, dtype=jnp.int32)[None, :, None, None] * OWNED
    return (chosen + worker).astype(jnp.int32)


def place_ends(result, stream_key, least, high):
    spot = [jax.random.randint(jax.random.fold_in(stream_key, axis), (), 0, length) for axis, length in enumerate(result.shape)]
    longest = result.shape.index(max(result.shape))
    next_to = spot[:longest] + [(spot[longest] + 1) % result.shape[longest]] + spot[longest + 1:]
    return result.at[tuple(spot)].set(least).at[tuple(next_to)].set(high)


def shard_levels(key, dims, pieces, smallest, top_value):
    def one(position, blocks):
        heights = jax.random.uniform(jax.random.fold_in(jax.random.fold_in(key, 6), position), (blocks,), jnp.float32, smallest / len(pieces), top_value / len(pieces))
        return jnp.repeat(jnp.exp(heights), dims[position] // blocks).reshape((-1,) + (1,) * (len(dims) - position - 1))

    factor_of = one(*pieces[0])
    for cut in pieces[1:]:
        factor_of = factor_of * one(*cut)
    return factor_of


def noise(own_key, shape, width, limit, split=(), kind=jnp.bfloat16):
    level = shard_levels(own_key, shape, split, -0.22, 0.18) if split else 1.0
    result = jax.random.normal(own_key, shape, jnp.float32) * width * level
    return jnp.minimum(jnp.maximum(result, -limit), limit).astype(kind)


def setup_inputs(seed: int = 0) -> dict:
    arg_keys = jax.random.split(jax.random.key(seed), 5)
    return {
        "embeds": noise(arg_keys[0], (BLOCKS, BLOCK, D), 1.0, 6.0, ((0, 64), (1, 4))),
        "fetch_list": draw_fetch_list(jax.random.fold_in(arg_keys[4], 71), 0),
        "partners": draw_partners(jax.random.fold_in(arg_keys[4], 71), 0),
        "counts": place_ends(jax.random.randint(arg_keys[3], (BLOCKS,), BLOCK // 4, BLOCK + 1), jax.random.fold_in(arg_keys[3], 1), BLOCK // 4, BLOCK).astype(jnp.int32),
    }


EPS = 1e-06

def reference(embeds, fetch_list, partners, counts):
    values = embeds.astype(jnp.float32)
    unit = (values * lax.rsqrt(lax.optimization_barrier(jnp.sum(values * values, axis=-1, keepdims=True)) + EPS)).astype(jnp.bfloat16)
    positions = jnp.arange(embeds.shape[1], dtype=jnp.int32)
    valid = positions[None, :] < counts[:, None]
    lenders = fetch_list.reshape(-1, fetch_list.shape[-1])
    listed = partners.reshape(-1, partners.shape[2], partners.shape[3])
    lanes = jnp.arange(N_GY, dtype=jnp.int32)[:, None] * QUARTER + jnp.arange(SLICE, dtype=jnp.int32)[None, :]
    lanes = lanes.reshape(-1)

    def advance(best, entries):
        tiles, partner_ids = entries
        lent_ids = (tiles // PIECES).astype(jnp.int32)
        piece_ids = (tiles % PIECES).astype(jnp.int32)
        rows = (piece_ids[:, None] * SLICE + lanes[None, :]).astype(jnp.int32)
        owners = jnp.broadcast_to(lent_ids[:, None], rows.shape)
        left = unit[owners, rows].astype(jnp.float32)
        right = unit[partner_ids].astype(jnp.float32)
        scores = jnp.einsum('gqd,gkbd->gqkb', left, right)
        row_ok = rows < counts[lent_ids][:, None]
        keep = row_ok[:, :, None, None] & valid[partner_ids][:, None, :, :]
        scores = jnp.where(keep, scores, jnp.float32(-1.0))
        best = best.at[owners, rows].max(lax.optimization_barrier(jnp.max(scores, axis=(2, 3))))
        best = best.at[partner_ids].max(lax.optimization_barrier(jnp.max(scores, axis=1)))
        return (best, None)
    start = jnp.full(valid.shape, -1.0, jnp.float32)
    best, _ = lax.scan(advance, start, (lenders, listed))
    return jnp.where(valid, best, jnp.float32(-1.0))
```

```python
import jax
import jax.numpy as jnp
from jax import lax
from jax.sharding import PartitionSpec as P

SLICE = 8


EPS = 1e-06


def normalize(source):
    values = source.astype(jnp.float32)
    return (values * lax.rsqrt(jnp.sum(values * values, axis=-1, keepdims=True) + EPS)).astype(
        jnp.bfloat16
    )


def lent_scores(lent, row_valid, listed, own_unit, col_valid):
    slots, lanes, lent_rows, width = lent.shape
    owned, quarter, _ = own_unit.shape
    flat_rows = lent.reshape(slots * lanes * lent_rows, width)
    scores = jnp.einsum("rd,kcd->rkc", flat_rows, own_unit, preferred_element_type=jnp.float32)
    scores = scores.reshape(slots, lanes, lent_rows, owned, quarter)
    keep = (
        row_valid[:, :, :, None, None]
        & listed[:, None, None, :, None]
        & col_valid[None, None, None, :, :]
    )
    scores = jnp.where(keep, scores, jnp.float32(-1.0))
    return jnp.max(scores, axis=(3, 4)), jnp.max(scores, axis=(0, 1, 2))


def on_device(embeds, fetch_list, partners, counts):
    owned, quarter, width = embeds.shape
    slice_rows = SLICE
    pieces = quarter // slice_rows
    my_group = lax.axis_index("gx")
    my_lane = lax.axis_index("gy")
    n_gy = lax.axis_size("gy")
    first = my_group * owned
    waves = fetch_list.shape[0]
    own_unit = normalize(embeds)
    own_pieces = own_unit.reshape(owned, pieces, slice_rows, width)
    own_counts = lax.dynamic_slice_in_dim(counts, first, owned)
    col_positions = my_lane * quarter + jnp.arange(quarter, dtype=jnp.int32)
    col_valid = col_positions[None, :] < own_counts[:, None]
    lane_rows = (
        jnp.arange(n_gy, dtype=jnp.int32)[:, None] * quarter
        + jnp.arange(slice_rows, dtype=jnp.int32)[None, :]
    )
    local_ids = jnp.arange(owned, dtype=jnp.int32)
    piece_ids = jnp.arange(pieces, dtype=jnp.int32)
    col_total = jnp.full((owned, quarter), -1.0, jnp.float32)
    row_parts = []
    sent_blocks = []
    sent_pieces = []
    for wave_index in range(waves):
        tiles = lax.dynamic_index_in_dim(fetch_list[wave_index], my_group, 1, False)
        outgoing_sent_block = tiles // pieces - first
        outgoing_sent_piece = tiles % pieces
        sent_blocks.append(outgoing_sent_block)
        sent_pieces.append(outgoing_sent_piece)
        outbound = own_pieces[outgoing_sent_block, outgoing_sent_piece]
        arrived = lax.all_to_all(outbound, "gx", split_axis=0, concat_axis=0, tiled=True)
        lent = lax.all_gather(arrived, "gy", axis=1, tiled=False)
        incoming = lax.dynamic_index_in_dim(fetch_list[wave_index], my_group, 0, False)
        arrived_counts = counts[incoming // pieces]
        arrived_rows = (incoming % pieces)[:, None, None] * slice_rows + lane_rows[None, :, :]
        row_valid = arrived_rows < arrived_counts[:, None, None]
        chosen = lax.dynamic_index_in_dim(partners[wave_index], my_group, 0, False) - first
        listed = jnp.any(chosen[:, :, None] == local_ids[None, None, :], axis=1)
        row_best, col_best = lent_scores(lent, row_valid, listed, own_unit, col_valid)
        row_parts.append(row_best)
        col_total = jnp.maximum(col_total, col_best)
    row_all = jnp.stack(row_parts, axis=0)
    groups = row_all.shape[1]
    outgoing = jnp.transpose(row_all, (1, 2, 0, 3)).reshape(groups * n_gy, waves, slice_rows)
    returned = lax.all_to_all(outgoing, ("gx", "gy"), split_axis=0, concat_axis=0, tiled=True)
    returned = jnp.max(returned.reshape(groups, n_gy, waves, slice_rows), axis=1)
    row_total = jnp.full((owned, pieces, slice_rows), -1.0, jnp.float32)
    for wave_index in range(waves):
        match = (sent_blocks[wave_index][:, None, None] == local_ids[None, :, None]) & (
            sent_pieces[wave_index][:, None, None] == piece_ids[None, None, :]
        )
        placed = jnp.max(
            jnp.where(
                match[:, :, :, None], returned[:, wave_index][:, None, None, :], jnp.float32(-1.0)
            ),
            axis=0,
        )
        row_total = jnp.maximum(row_total, placed)
    nearest = jnp.maximum(row_total.reshape(owned, quarter), col_total)
    mine_valid = col_positions[None, :] < own_counts[:, None]
    return jnp.where(mine_valid, nearest, jnp.float32(-1.0))


def solution(mesh):
    in_specs = (P("gx", "gy", None), P(), P(), P())
    out_specs = P("gx", "gy")
    return jax.shard_map(
        on_device, mesh=mesh, in_specs=in_specs, out_specs=out_specs, check_vma=False
    )
```

```python
import jax
import jax.numpy as jnp
from jax import lax
from jax.experimental import pallas as pl
from jax.experimental.pallas import tpu as pltpu
from jax.sharding import PartitionSpec as P

SLICE = 8


EPS = 1e-06


def normalize(source):
    values = source.astype(jnp.float32)
    return (values * lax.rsqrt(jnp.sum(values * values, axis=-1, keepdims=True) + EPS)).astype(
        jnp.bfloat16
    )


def _score_kernel(rowmask_ref, colvalid_ref, lhs_ref, rhs_ref, rowmax_ref, colmax_ref):
    step = pl.program_id(0)
    scores = lax.dot_general(
        lhs_ref[...], rhs_ref[...], (((1,), (1,)), ((), ())), preferred_element_type=jnp.float32
    )
    keep = (rowmask_ref[0] > 0) & (colvalid_ref[0] > 0)
    scores = jnp.where(keep, scores, jnp.float32(-1.0))
    row_best = jnp.max(scores, axis=1, keepdims=True)
    colmax_ref[0] = jnp.max(scores, axis=0, keepdims=True)

    @pl.when(step == 0)
    def _():
        rowmax_ref[...] = jnp.broadcast_to(row_best, rowmax_ref.shape)

    @pl.when(step > 0)
    def _():
        rowmax_ref[...] = jnp.maximum(rowmax_ref[...], row_best)


def lent_scores(lent, row_valid, listed, columns, col_valid):
    slots, lent_rows, width = lent.shape
    owned, quarter, _ = columns.shape
    n_rows = slots * lent_rows
    tiles = owned
    flat_rows = lent.reshape(n_rows, width)
    flat_cols = columns.reshape(tiles * quarter, width)
    rowmask = (row_valid[None, :, :] & jnp.transpose(listed)[:, :, None]).astype(jnp.int32)
    rowmask = rowmask.reshape(owned, n_rows, 1)
    colmask = col_valid.astype(jnp.int32).reshape(tiles, 1, quarter)
    rowmax, colmax = pl.pallas_call(
        _score_kernel,
        out_shape=(
            jax.ShapeDtypeStruct((n_rows, 128), jnp.float32),
            jax.ShapeDtypeStruct((tiles, 1, quarter), jnp.float32),
        ),
        grid=(tiles,),
        in_specs=[
            pl.BlockSpec((1, n_rows, 1), lambda j: (j, 0, 0)),
            pl.BlockSpec((1, 1, quarter), lambda j: (j, 0, 0)),
            pl.BlockSpec((n_rows, width), lambda j: (0, 0)),
            pl.BlockSpec((quarter, width), lambda j: (j, 0)),
        ],
        out_specs=[
            pl.BlockSpec((n_rows, 128), lambda j: (0, 0)),
            pl.BlockSpec((1, 1, quarter), lambda j: (j, 0, 0)),
        ],
        compiler_params=pltpu.CompilerParams(dimension_semantics=("arbitrary",)),
        cost_estimate=pl.CostEstimate(
            flops=2 * n_rows * tiles * quarter * width,
            transcendentals=0,
            bytes_accessed=2 * (n_rows + tiles * quarter) * width,
        ),
    )(rowmask, colmask, flat_rows, flat_cols)
    return rowmax[:, 0].reshape(slots, lent_rows), colmax.reshape(owned, quarter)


def on_device(embeds, fetch_list, partners, counts):
    owned, quarter, width = embeds.shape
    slice_rows = SLICE
    pieces = quarter // slice_rows
    my_group = lax.axis_index("gx")
    my_lane = lax.axis_index("gy")
    n_gy = lax.axis_size("gy")
    first = my_group * owned
    waves = fetch_list.shape[0]
    pair_p = [(lane, lane ^ 1) for lane in range(n_gy)]
    pair_r = [(lane, n_gy - 1 - lane) for lane in range(n_gy)]
    lane_p = jnp.bitwise_xor(my_lane, 1)
    lane_r = n_gy - 1 - my_lane
    own_unit = normalize(embeds)
    other_unit = lax.ppermute(own_unit, "gy", pair_p)
    own_pieces = own_unit.reshape(owned, pieces, slice_rows, width)
    own_counts = lax.dynamic_slice_in_dim(counts, first, owned)
    positions = jnp.arange(quarter, dtype=jnp.int32)
    col_sources = []
    for lane, unit in ((my_lane, own_unit), (lane_p, other_unit)):
        col_valid = (lane * quarter + positions)[None, :] < own_counts[:, None]
        col_sources.append((unit, col_valid))
    slice_offsets = jnp.arange(slice_rows, dtype=jnp.int32)
    local_ids = jnp.arange(owned, dtype=jnp.int32)
    piece_ids = jnp.arange(pieces, dtype=jnp.int32)
    col_part = [jnp.full((owned, quarter), -1.0, jnp.float32) for _ in col_sources]
    row_mine_parts = []
    row_other_parts = []
    sent_blocks = []
    sent_pieces = []
    for wave_index in range(waves):
        tiles = lax.dynamic_index_in_dim(fetch_list[wave_index], my_group, 1, False)
        outgoing_sent_block = tiles // pieces - first
        outgoing_sent_piece = tiles % pieces
        sent_blocks.append(outgoing_sent_block)
        sent_pieces.append(outgoing_sent_piece)
        outbound = own_pieces[outgoing_sent_block, outgoing_sent_piece]
        arrived = lax.all_to_all(outbound, "gx", split_axis=0, concat_axis=0, tiled=True)
        arrived_other = lax.ppermute(arrived, "gy", pair_r)
        incoming = lax.dynamic_index_in_dim(fetch_list[wave_index], my_group, 0, False)
        arrived_counts = counts[incoming // pieces]
        chosen = lax.dynamic_index_in_dim(partners[wave_index], my_group, 0, False) - first
        listed = jnp.any(chosen[:, :, None] == local_ids[None, None, :], axis=1)
        piece_rows = (incoming % pieces)[:, None] * slice_rows + slice_offsets[None, :]
        for lane, rows_in, parts in (
            (my_lane, arrived, row_mine_parts),
            (lane_r, arrived_other, row_other_parts),
        ):
            row_valid = (lane * quarter + piece_rows) < arrived_counts[:, None]
            row_best = jnp.full(row_valid.shape, -1.0, jnp.float32)
            for source, (unit, col_valid) in enumerate(col_sources):
                rows_max, col_best = lent_scores(rows_in, row_valid, listed, unit, col_valid)
                row_best = jnp.maximum(row_best, rows_max)
                col_part[source] = jnp.maximum(col_part[source], col_best)
            parts.append(row_best)
    col_back = lax.ppermute(col_part[1], "gy", pair_p)
    col_total = jnp.maximum(col_part[0], col_back)
    row_other = jnp.stack(row_other_parts, axis=0)
    row_back = lax.ppermute(row_other, "gy", pair_r)
    row_mine = jnp.maximum(jnp.stack(row_mine_parts, axis=0), row_back)
    returned = lax.all_to_all(row_mine, "gx", split_axis=1, concat_axis=1, tiled=True)
    row_total = jnp.full((owned, pieces, slice_rows), -1.0, jnp.float32)
    for wave_index in range(waves):
        match = (sent_blocks[wave_index][:, None, None] == local_ids[None, :, None]) & (
            sent_pieces[wave_index][:, None, None] == piece_ids[None, None, :]
        )
        placed = jnp.max(
            jnp.where(
                match[:, :, :, None], returned[wave_index][:, None, None, :], jnp.float32(-1.0)
            ),
            axis=0,
        )
        row_total = jnp.maximum(row_total, placed)
    nearest = jnp.maximum(row_total.reshape(owned, quarter), col_total)
    mine_valid = (my_lane * quarter + positions)[None, :] < own_counts[:, None]
    return jnp.where(mine_valid, nearest, jnp.float32(-1.0))


def solution(mesh):
    in_specs = (P("gx", "gy", None), P(), P(), P())
    out_specs = P("gx", "gy")
    return jax.shard_map(
        on_device, mesh=mesh, in_specs=in_specs, out_specs=out_specs, check_vma=False
    )
```

```python
import jax
import jax.numpy as jnp
from jax import lax
from jax.experimental import pallas as pl
from jax.experimental.pallas import tpu as pltpu
from jax.sharding import PartitionSpec as P

SLICE = 8


EPS = 1e-06


def normalize(source):
    values = source.astype(jnp.float32)
    return (values * lax.rsqrt(jnp.sum(values * values, axis=-1, keepdims=True) + EPS)).astype(
        jnp.bfloat16
    )


def _score_kernel(limit_ref, rowmask_ref, lhs_ref, rhs_ref, rowmax_ref, colmax_ref, acc_ref):
    step = pl.program_id(0)
    scores = lax.dot_general(
        lhs_ref[...], rhs_ref[0], (((1,), (1,)), ((), ())), preferred_element_type=jnp.float32
    )
    n_rows, n_cols = scores.shape
    lanes = rowmask_ref.shape[-1]
    row_keep = rowmask_ref[0] > 0
    row_keep = jnp.concatenate([row_keep] * (n_cols // lanes), axis=1)
    col_keep = lax.broadcasted_iota(jnp.int32, (1, n_cols), 1) < limit_ref[step]
    scores = jnp.where(row_keep & col_keep, scores, jnp.float32(-1.0))
    colmax_ref[0] = jnp.max(scores, axis=0, keepdims=True)
    part = scores[:, 0:lanes]
    for start in range(lanes, n_cols, lanes):
        part = jnp.maximum(part, scores[:, start : start + lanes])

    @pl.when(step == 0)
    def _():
        acc_ref[...] = part

    @pl.when(step > 0)
    def _():
        acc_ref[...] = jnp.maximum(acc_ref[...], part)

    @pl.when(step == pl.num_programs(0) - 1)
    def _():
        rowmax_ref[...] = jnp.broadcast_to(
            jnp.max(acc_ref[...], axis=1, keepdims=True), rowmax_ref.shape
        )


def lent_scores(lent, row_valid, listed, columns, col_limit):
    slots, lent_rows, width = lent.shape
    owned, quarter, _ = columns.shape
    n_rows = slots * lent_rows
    lanes = 128
    flat_rows = lent.reshape(n_rows, width)
    rowmask = (row_valid[None, :, :] & jnp.transpose(listed)[:, :, None]).astype(jnp.int32)
    rowmask = jnp.broadcast_to(rowmask.reshape(owned, n_rows, 1), (owned, n_rows, lanes))
    rowmax, colmax = pl.pallas_call(
        _score_kernel,
        out_shape=(
            jax.ShapeDtypeStruct((n_rows, lanes), jnp.float32),
            jax.ShapeDtypeStruct((owned, 1, quarter), jnp.float32),
        ),
        grid_spec=pltpu.PrefetchScalarGridSpec(
            num_scalar_prefetch=1,
            grid=(owned,),
            in_specs=[
                pl.BlockSpec((1, n_rows, lanes), lambda k, lim: (k, 0, 0)),
                pl.BlockSpec((n_rows, width), lambda k, lim: (0, 0)),
                pl.BlockSpec((1, quarter, width), lambda k, lim: (k, 0, 0)),
            ],
            out_specs=[
                pl.BlockSpec((n_rows, lanes), lambda k, lim: (0, 0)),
                pl.BlockSpec((1, 1, quarter), lambda k, lim: (k, 0, 0)),
            ],
            scratch_shapes=[pltpu.VMEM((n_rows, lanes), jnp.float32)],
        ),
        compiler_params=pltpu.CompilerParams(dimension_semantics=("arbitrary",)),
        cost_estimate=pl.CostEstimate(
            flops=2 * n_rows * owned * quarter * width,
            transcendentals=0,
            bytes_accessed=2 * (n_rows + owned * quarter) * width + 4 * owned * n_rows * lanes,
        ),
    )(col_limit, rowmask, flat_rows, columns)
    return rowmax[:, 0].reshape(slots, lent_rows), colmax.reshape(owned, quarter)


def on_device(embeds, fetch_list, partners, counts):
    owned, quarter, width = embeds.shape
    slice_rows = SLICE
    pieces = quarter // slice_rows
    my_group = lax.axis_index("gx")
    my_lane = lax.axis_index("gy")
    n_gy = lax.axis_size("gy")
    first = my_group * owned
    waves = fetch_list.shape[0]
    pair_p = [(lane, lane ^ 1) for lane in range(n_gy)]
    pair_r = [(lane, n_gy - 1 - lane) for lane in range(n_gy)]
    lane_p = jnp.bitwise_xor(my_lane, 1)
    lane_r = n_gy - 1 - my_lane
    own_unit = normalize(embeds)
    other_unit = lax.ppermute(own_unit, "gy", pair_p)
    own_pieces = own_unit.reshape(owned, pieces, slice_rows, width)
    own_counts = lax.dynamic_slice_in_dim(counts, first, owned)
    positions = jnp.arange(quarter, dtype=jnp.int32)
    col_sources = []
    for lane, unit in ((my_lane, own_unit), (lane_p, other_unit)):
        col_limit = (own_counts - lane * quarter).astype(jnp.int32)
        col_sources.append((unit, col_limit))
    slice_offsets = jnp.arange(slice_rows, dtype=jnp.int32)
    local_ids = jnp.arange(owned, dtype=jnp.int32)
    piece_ids = jnp.arange(pieces, dtype=jnp.int32)
    col_part = [jnp.full((owned, quarter), -1.0, jnp.float32) for _ in col_sources]
    row_mine_parts = []
    row_other_parts = []
    sent_blocks = []
    sent_pieces = []
    for wave_index in range(waves):
        tiles = lax.dynamic_index_in_dim(fetch_list[wave_index], my_group, 1, False)
        outgoing_sent_block = tiles // pieces - first
        outgoing_sent_piece = tiles % pieces
        sent_blocks.append(outgoing_sent_block)
        sent_pieces.append(outgoing_sent_piece)
        outbound = own_pieces[outgoing_sent_block, outgoing_sent_piece]
        arrived = lax.all_to_all(outbound, "gx", split_axis=0, concat_axis=0, tiled=True)
        arrived_other = lax.ppermute(arrived, "gy", pair_r)
        incoming = lax.dynamic_index_in_dim(fetch_list[wave_index], my_group, 0, False)
        arrived_counts = counts[incoming // pieces]
        chosen = lax.dynamic_index_in_dim(partners[wave_index], my_group, 0, False) - first
        listed = jnp.any(chosen[:, :, None] == local_ids[None, None, :], axis=1)
        piece_rows = (incoming % pieces)[:, None] * slice_rows + slice_offsets[None, :]
        for lane, rows_in, parts in (
            (my_lane, arrived, row_mine_parts),
            (lane_r, arrived_other, row_other_parts),
        ):
            row_valid = (lane * quarter + piece_rows) < arrived_counts[:, None]
            row_best = jnp.full(row_valid.shape, -1.0, jnp.float32)
            for source, (unit, col_limit) in enumerate(col_sources):
                rows_max, col_best = lent_scores(rows_in, row_valid, listed, unit, col_limit)
                row_best = jnp.maximum(row_best, rows_max)
                col_part[source] = jnp.maximum(col_part[source], col_best)
            parts.append(row_best)
    col_back = lax.ppermute(col_part[1], "gy", pair_p)
    col_total = jnp.maximum(col_part[0], col_back)
    row_other = jnp.stack(row_other_parts, axis=0)
    row_back = lax.ppermute(row_other, "gy", pair_r)
    row_mine = jnp.maximum(jnp.stack(row_mine_parts, axis=0), row_back)
    returned = lax.all_to_all(row_mine, "gx", split_axis=1, concat_axis=1, tiled=True)
    row_total = jnp.full((owned, pieces, slice_rows), -1.0, jnp.float32)
    for wave_index in range(waves):
        match = (sent_blocks[wave_index][:, None, None] == local_ids[None, :, None]) & (
            sent_pieces[wave_index][:, None, None] == piece_ids[None, None, :]
        )
        placed = jnp.max(
            jnp.where(
                match[:, :, :, None], returned[wave_index][:, None, None, :], jnp.float32(-1.0)
            ),
            axis=0,
        )
        row_total = jnp.maximum(row_total, placed)
    nearest = jnp.maximum(row_total.reshape(owned, quarter), col_total)
    mine_valid = (my_lane * quarter + positions)[None, :] < own_counts[:, None]
    return jnp.where(mine_valid, nearest, jnp.float32(-1.0))


def solution(mesh):
    in_specs = (P("gx", "gy", None), P(), P(), P())
    out_specs = P("gx", "gy")
    return jax.shard_map(
        on_device, mesh=mesh, in_specs=in_specs, out_specs=out_specs, check_vma=False
    )
```

```python
import jax
import jax.numpy as jnp
from jax import lax
from jax.sharding import PartitionSpec as P

SLICE = 8


EPS = 1e-06


def normalize(source):
    values = source.astype(jnp.float32)
    return (values * lax.rsqrt(jnp.sum(values * values, axis=-1, keepdims=True) + EPS)).astype(
        jnp.bfloat16
    )


def lent_scores(lent, row_valid, listed, columns, col_limit):
    slots, lent_rows, width = lent.shape
    owned, quarter, _ = columns.shape
    flat_rows = lent.reshape(slots * lent_rows, width)
    scores = jnp.einsum("rd,kcd->rkc", flat_rows, columns, preferred_element_type=jnp.float32)
    scores = scores.reshape(slots, lent_rows, owned, quarter)
    col_valid = jnp.arange(quarter, dtype=jnp.int32)[None, :] < col_limit[:, None]
    keep = row_valid[:, :, None, None] & listed[:, None, :, None] & col_valid[None, None, :, :]
    scores = jnp.where(keep, scores, jnp.float32(-1.0))
    return jnp.max(scores, axis=(2, 3)), jnp.max(scores, axis=(0, 1))


def on_device(embeds, fetch_list, partners, counts):
    owned, quarter, width = embeds.shape
    slice_rows = SLICE
    pieces = quarter // slice_rows
    my_group = lax.axis_index("gx")
    my_lane = lax.axis_index("gy")
    n_gy = lax.axis_size("gy")
    first = my_group * owned
    waves = fetch_list.shape[0]
    pair_p = [(lane, lane ^ 1) for lane in range(n_gy)]
    pair_r = [(lane, n_gy - 1 - lane) for lane in range(n_gy)]
    lane_p = jnp.bitwise_xor(my_lane, 1)
    lane_r = n_gy - 1 - my_lane
    own_unit = normalize(embeds)
    other_unit = lax.ppermute(own_unit, "gy", pair_p)
    own_pieces = own_unit.reshape(owned, pieces, slice_rows, width)
    own_counts = lax.dynamic_slice_in_dim(counts, first, owned)
    positions = jnp.arange(quarter, dtype=jnp.int32)
    col_sources = []
    for lane, unit in ((my_lane, own_unit), (lane_p, other_unit)):
        col_limit = (own_counts - lane * quarter).astype(jnp.int32)
        col_sources.append((unit, col_limit))
    slice_offsets = jnp.arange(slice_rows, dtype=jnp.int32)
    local_ids = jnp.arange(owned, dtype=jnp.int32)
    piece_ids = jnp.arange(pieces, dtype=jnp.int32)
    col_part = [jnp.full((owned, quarter), -1.0, jnp.float32) for _ in col_sources]
    row_mine_parts = []
    row_other_parts = []
    sent_blocks = []
    sent_pieces = []
    for wave_index in range(waves):
        tiles = lax.dynamic_index_in_dim(fetch_list[wave_index], my_group, 1, False)
        outgoing_sent_block = tiles // pieces - first
        outgoing_sent_piece = tiles % pieces
        sent_blocks.append(outgoing_sent_block)
        sent_pieces.append(outgoing_sent_piece)
        outbound = own_pieces[outgoing_sent_block, outgoing_sent_piece]
        arrived = lax.all_to_all(outbound, "gx", split_axis=0, concat_axis=0, tiled=True)
        arrived_other = lax.ppermute(arrived, "gy", pair_r)
        incoming = lax.dynamic_index_in_dim(fetch_list[wave_index], my_group, 0, False)
        arrived_counts = counts[incoming // pieces]
        chosen = lax.dynamic_index_in_dim(partners[wave_index], my_group, 0, False) - first
        listed = jnp.any(chosen[:, :, None] == local_ids[None, None, :], axis=1)
        piece_rows = (incoming % pieces)[:, None] * slice_rows + slice_offsets[None, :]
        for lane, rows_in, parts in (
            (my_lane, arrived, row_mine_parts),
            (lane_r, arrived_other, row_other_parts),
        ):
            row_valid = (lane * quarter + piece_rows) < arrived_counts[:, None]
            row_best = jnp.full(row_valid.shape, -1.0, jnp.float32)
            for source, (unit, col_limit) in enumerate(col_sources):
                rows_max, col_best = lent_scores(rows_in, row_valid, listed, unit, col_limit)
                row_best = jnp.maximum(row_best, rows_max)
                col_part[source] = jnp.maximum(col_part[source], col_best)
            parts.append(row_best)
    col_back = lax.ppermute(col_part[1], "gy", pair_p)
    col_total = jnp.maximum(col_part[0], col_back)
    row_other = jnp.stack(row_other_parts, axis=0)
    row_back = lax.ppermute(row_other, "gy", pair_r)
    row_mine = jnp.maximum(jnp.stack(row_mine_parts, axis=0), row_back)
    returned = lax.all_to_all(row_mine, "gx", split_axis=1, concat_axis=1, tiled=True)
    row_total = jnp.full((owned, pieces, slice_rows), -1.0, jnp.float32)
    for wave_index in range(waves):
        match = (sent_blocks[wave_index][:, None, None] == local_ids[None, :, None]) & (
            sent_pieces[wave_index][:, None, None] == piece_ids[None, None, :]
        )
        placed = jnp.max(
            jnp.where(
                match[:, :, :, None], returned[wave_index][:, None, None, :], jnp.float32(-1.0)
            ),
            axis=0,
        )
        row_total = jnp.maximum(row_total, placed)
    nearest = jnp.maximum(row_total.reshape(owned, quarter), col_total)
    mine_valid = (my_lane * quarter + positions)[None, :] < own_counts[:, None]
    return jnp.where(mine_valid, nearest, jnp.float32(-1.0))


def solution(mesh):
    in_specs = (P("gx", "gy", None), P(), P(), P())
    out_specs = P("gx", "gy")
    return jax.shard_map(
        on_device, mesh=mesh, in_specs=in_specs, out_specs=out_specs, check_vma=False
    )
```

```python
import jax
import jax.numpy as jnp
from jax import lax
from jax.sharding import PartitionSpec as P


SLICE = 8


EPS = 1e-06


def normalize(source):
    values = source.astype(jnp.float32)
    return (values * lax.rsqrt(jnp.sum(values * values, axis=-1, keepdims=True) + EPS)).astype(
        jnp.bfloat16
    )


def lent_scores(lent, row_valid, listed, columns, col_limit):
    slots, lent_rows, width = lent.shape
    owned, quarter, _ = columns.shape
    flat_rows = lent.reshape(slots * lent_rows, width)
    scores = jnp.einsum("rd,kcd->rkc", flat_rows, columns, preferred_element_type=jnp.float32)
    scores = scores.reshape(slots, lent_rows, owned, quarter)
    col_valid = jnp.arange(quarter, dtype=jnp.int32)[None, :] < col_limit[:, None]
    keep = row_valid[:, :, None, None] & listed[:, None, :, None] & col_valid[None, None, :, :]
    scores = jnp.where(keep, scores, jnp.float32(-1.0))
    return jnp.max(scores, axis=(2, 3)), jnp.max(scores, axis=(0, 1))


def device_body(embeds, fetch_list, partners, counts):
    owned, quarter, width = embeds.shape
    slice_rows = SLICE
    pieces = quarter // slice_rows
    my_group = lax.axis_index("gx")
    my_lane = lax.axis_index("gy")
    n_gy = lax.axis_size("gy")
    first = my_group * owned
    waves = fetch_list.shape[0]
    pair_p = [(lane, lane ^ 1) for lane in range(n_gy)]
    pair_r = [(lane, n_gy - 1 - lane) for lane in range(n_gy)]
    lane_p = jnp.bitwise_xor(my_lane, 1)
    lane_r = n_gy - 1 - my_lane
    own_unit = normalize(embeds)
    other_unit = lax.ppermute(own_unit, "gy", pair_p)
    own_pieces = own_unit.reshape(owned, pieces, slice_rows, width)
    own_counts = lax.dynamic_slice_in_dim(counts, first, owned)
    positions = jnp.arange(quarter, dtype=jnp.int32)
    col_sources = []
    for lane, unit in ((my_lane, own_unit), (lane_p, other_unit)):
        col_limit = (own_counts - lane * quarter).astype(jnp.int32)
        col_sources.append((unit, col_limit))
    slice_offsets = jnp.arange(slice_rows, dtype=jnp.int32)
    local_ids = jnp.arange(owned, dtype=jnp.int32)
    piece_ids = jnp.arange(pieces, dtype=jnp.int32)
    col_part = [jnp.full((owned, quarter), -1.0, jnp.float32) for _ in col_sources]
    sent_blocks = []
    sent_pieces = []
    jobs = []
    for wave_index in range(waves):
        tiles = lax.dynamic_index_in_dim(fetch_list[wave_index], my_group, 1, False)
        outgoing_sent_block = tiles // pieces - first
        outgoing_sent_piece = tiles % pieces
        sent_blocks.append(outgoing_sent_block)
        sent_pieces.append(outgoing_sent_piece)
        outbound = own_pieces[outgoing_sent_block, outgoing_sent_piece]
        arrived = lax.all_to_all(outbound, "gx", split_axis=0, concat_axis=0, tiled=True)
        arrived_other = lax.ppermute(arrived, "gy", pair_r)
        incoming = lax.dynamic_index_in_dim(fetch_list[wave_index], my_group, 0, False)
        arrived_counts = counts[incoming // pieces]
        chosen = lax.dynamic_index_in_dim(partners[wave_index], my_group, 0, False) - first
        listed = jnp.any(chosen[:, :, None] == local_ids[None, None, :], axis=1)
        piece_rows = (incoming % pieces)[:, None] * slice_rows + slice_offsets[None, :]
        for part, (lane, rows_in) in enumerate(((my_lane, arrived), (lane_r, arrived_other))):
            row_valid = (lane * quarter + piece_rows) < arrived_counts[:, None]
            jobs.append((wave_index, part, rows_in, row_valid, listed))
    row_best = {}
    token = None
    for source, (unit, col_limit) in enumerate(col_sources):
        for wave_index, part, rows_in, row_valid, listed in jobs:
            if token is not None:
                token, rows_in, unit = lax.optimization_barrier((token, rows_in, unit))
            rows_max, col_best = lent_scores(rows_in, row_valid, listed, unit, col_limit)
            token = (rows_max, col_best)
            key = (wave_index, part)
            row_best[key] = rows_max if key not in row_best else jnp.maximum(row_best[key], rows_max)
            col_part[source] = jnp.maximum(col_part[source], col_best)
    row_mine_parts = [row_best[(wave_index, 0)] for wave_index in range(waves)]
    row_other_parts = [row_best[(wave_index, 1)] for wave_index in range(waves)]
    col_back = lax.ppermute(col_part[1], "gy", pair_p)
    col_total = jnp.maximum(col_part[0], col_back)
    row_other = jnp.stack(row_other_parts, axis=0)
    row_back = lax.ppermute(row_other, "gy", pair_r)
    row_mine = jnp.maximum(jnp.stack(row_mine_parts, axis=0), row_back)
    returned = lax.all_to_all(row_mine, "gx", split_axis=1, concat_axis=1, tiled=True)
    row_total = jnp.full((owned, pieces, slice_rows), -1.0, jnp.float32)
    for wave_index in range(waves):
        match = (sent_blocks[wave_index][:, None, None] == local_ids[None, :, None]) & (
            sent_pieces[wave_index][:, None, None] == piece_ids[None, None, :]
        )
        placed = jnp.max(
            jnp.where(
                match[:, :, :, None], returned[wave_index][:, None, None, :], jnp.float32(-1.0)
            ),
            axis=0,
        )
        row_total = jnp.maximum(row_total, placed)
    nearest = jnp.maximum(row_total.reshape(owned, quarter), col_total)
    mine_valid = (my_lane * quarter + positions)[None, :] < own_counts[:, None]
    return jnp.where(mine_valid, nearest, jnp.float32(-1.0))


def solution(mesh):
    in_specs = (P("gx", "gy", None), P(), P(), P())
    out_specs = P("gx", "gy")
    return jax.shard_map(
        device_body, mesh=mesh, in_specs=in_specs, out_specs=out_specs, check_vma=False
    )
```

```python
import jax
import jax.numpy as jnp
from jax import lax
from jax.sharding import PartitionSpec as P


SLICE = 8


EPS = 1e-06


def normalize(source):
    values = source.astype(jnp.float32)
    return (values * lax.rsqrt(jnp.sum(values * values, axis=-1, keepdims=True) + EPS)).astype(
        jnp.bfloat16
    )


def lent_scores(lent, row_valid, listed, columns, col_limit):
    slots, lent_rows, width = lent.shape
    owned, quarter, _ = columns.shape
    flat_rows = lent.reshape(slots * lent_rows, width)
    scores = jnp.einsum("rd,kcd->rkc", flat_rows, columns, preferred_element_type=jnp.float32)
    scores = scores.reshape(slots, lent_rows, owned, quarter)
    col_valid = jnp.arange(quarter, dtype=jnp.int32)[None, :] < col_limit[:, None]
    keep = row_valid[:, :, None, None] & listed[:, None, :, None] & col_valid[None, None, :, :]
    scores = jnp.where(keep, scores, jnp.float32(-1.0))
    return jnp.max(scores, axis=(2, 3)), jnp.max(scores, axis=(0, 1))


def device_body(embeds, fetch_list, partners, counts):
    owned, quarter, width = embeds.shape
    slice_rows = SLICE
    pieces = quarter // slice_rows
    my_group = lax.axis_index("gx")
    my_lane = lax.axis_index("gy")
    n_gy = lax.axis_size("gy")
    first = my_group * owned
    waves = fetch_list.shape[0]
    pair_p = [(lane, lane ^ 1) for lane in range(n_gy)]
    pair_r = [(lane, n_gy - 1 - lane) for lane in range(n_gy)]
    lane_p = jnp.bitwise_xor(my_lane, 1)
    lane_r = n_gy - 1 - my_lane
    own_unit = normalize(embeds)
    other_unit = lax.ppermute(own_unit, "gy", pair_p)
    own_pieces = own_unit.reshape(owned, pieces, slice_rows, width)
    own_counts = lax.dynamic_slice_in_dim(counts, first, owned)
    positions = jnp.arange(quarter, dtype=jnp.int32)
    col_sources = []
    for lane, unit in ((my_lane, own_unit), (lane_p, other_unit)):
        col_limit = (own_counts - lane * quarter).astype(jnp.int32)
        col_sources.append((unit, col_limit))
    slice_offsets = jnp.arange(slice_rows, dtype=jnp.int32)
    local_ids = jnp.arange(owned, dtype=jnp.int32)
    piece_ids = jnp.arange(pieces, dtype=jnp.int32)
    col_part = [jnp.full((owned, quarter), -1.0, jnp.float32) for _ in col_sources]
    sent_blocks = []
    sent_pieces = []
    jobs = []
    for wave_index in range(waves):
        tiles = lax.dynamic_index_in_dim(fetch_list[wave_index], my_group, 1, False)
        outgoing_sent_block = tiles // pieces - first
        outgoing_sent_piece = tiles % pieces
        sent_blocks.append(outgoing_sent_block)
        sent_pieces.append(outgoing_sent_piece)
        outbound = own_pieces[outgoing_sent_block, outgoing_sent_piece]
        arrived = lax.all_to_all(outbound, "gx", split_axis=0, concat_axis=0, tiled=True)
        arrived_other = lax.ppermute(arrived, "gy", pair_r)
        incoming = lax.dynamic_index_in_dim(fetch_list[wave_index], my_group, 0, False)
        arrived_counts = counts[incoming // pieces]
        chosen = lax.dynamic_index_in_dim(partners[wave_index], my_group, 0, False) - first
        listed = jnp.any(chosen[:, :, None] == local_ids[None, None, :], axis=1)
        piece_rows = (incoming % pieces)[:, None] * slice_rows + slice_offsets[None, :]
        for part, (lane, rows_in) in enumerate(((my_lane, arrived), (lane_r, arrived_other))):
            row_valid = (lane * quarter + piece_rows) < arrived_counts[:, None]
            jobs.append((wave_index, part, rows_in, row_valid, listed))
    row_best = {}
    token = None
    order = sorted(
        ((source, job) for source in range(len(col_sources)) for job in range(len(jobs))),
        key=lambda item: (jobs[item[1]][0] == waves - 1 and jobs[item[1]][1] == 1, item[0], item[1]),
    )
    for source, job in order:
        unit, col_limit = col_sources[source]
        wave_index, part, rows_in, row_valid, listed = jobs[job]
        if token is not None:
            token, rows_in, unit = lax.optimization_barrier((token, rows_in, unit))
        rows_max, col_best = lent_scores(rows_in, row_valid, listed, unit, col_limit)
        token = (rows_max, col_best)
        key = (wave_index, part)
        row_best[key] = rows_max if key not in row_best else jnp.maximum(row_best[key], rows_max)
        col_part[source] = jnp.maximum(col_part[source], col_best)
    row_mine_parts = [row_best[(wave_index, 0)] for wave_index in range(waves)]
    row_other_parts = [row_best[(wave_index, 1)] for wave_index in range(waves)]
    col_back = lax.ppermute(col_part[1], "gy", pair_p)
    col_total = jnp.maximum(col_part[0], col_back)
    row_other = jnp.stack(row_other_parts, axis=0)
    row_back = lax.ppermute(row_other, "gy", pair_r)
    row_mine = jnp.maximum(jnp.stack(row_mine_parts, axis=0), row_back)
    returned = lax.all_to_all(row_mine, "gx", split_axis=1, concat_axis=1, tiled=True)
    row_total = jnp.full((owned, pieces, slice_rows), -1.0, jnp.float32)
    for wave_index in range(waves):
        match = (sent_blocks[wave_index][:, None, None] == local_ids[None, :, None]) & (
            sent_pieces[wave_index][:, None, None] == piece_ids[None, None, :]
        )
        placed = jnp.max(
            jnp.where(
                match[:, :, :, None], returned[wave_index][:, None, None, :], jnp.float32(-1.0)
            ),
            axis=0,
        )
        row_total = jnp.maximum(row_total, placed)
    nearest = jnp.maximum(row_total.reshape(owned, quarter), col_total)
    mine_valid = (my_lane * quarter + positions)[None, :] < own_counts[:, None]
    return jnp.where(mine_valid, nearest, jnp.float32(-1.0))


def solution(mesh):
    in_specs = (P("gx", "gy", None), P(), P(), P())
    out_specs = P("gx", "gy")
    return jax.shard_map(
        device_body, mesh=mesh, in_specs=in_specs, out_specs=out_specs, check_vma=False
    )
```

```python
import jax
import jax.numpy as jnp
from jax import lax
from jax.experimental import pallas as pl
from jax.experimental.pallas import tpu as pltpu
from jax.sharding import PartitionSpec as P


SLICE = 8


EPS = 1e-06


def _normalize_kernel(source_ref, unit_ref):
    values = source_ref[0].astype(jnp.float32)
    scale = lax.rsqrt(jnp.sum(values * values, axis=-1, keepdims=True) + EPS)
    unit_ref[0] = (values * scale).astype(unit_ref.dtype)


def normalize(source):
    owned, rows, width = source.shape
    return pl.pallas_call(
        _normalize_kernel,
        out_shape=jax.ShapeDtypeStruct(source.shape, jnp.bfloat16),
        grid=(owned,),
        in_specs=[pl.BlockSpec((1, rows, width), lambda k: (k, 0, 0))],
        out_specs=pl.BlockSpec((1, rows, width), lambda k: (k, 0, 0)),
        compiler_params=pltpu.CompilerParams(dimension_semantics=("arbitrary",)),
        cost_estimate=pl.CostEstimate(
            flops=3 * source.size, transcendentals=owned * rows, bytes_accessed=4 * source.size
        ),
    )(source)


def lent_scores(lent, row_valid, listed, columns, col_limit):
    slots, lent_rows, width = lent.shape
    owned, quarter, _ = columns.shape
    flat_rows = lent.reshape(slots * lent_rows, width)
    scores = jnp.einsum("rd,kcd->rkc", flat_rows, columns, preferred_element_type=jnp.float32)
    scores = scores.reshape(slots, lent_rows, owned, quarter)
    col_valid = jnp.arange(quarter, dtype=jnp.int32)[None, :] < col_limit[:, None]
    keep = row_valid[:, :, None, None] & listed[:, None, :, None] & col_valid[None, None, :, :]
    scores = jnp.where(keep, scores, jnp.float32(-1.0))
    return jnp.max(scores, axis=(2, 3)), jnp.max(scores, axis=(0, 1))


def device_body(embeds, fetch_list, partners, counts):
    owned, quarter, width = embeds.shape
    slice_rows = SLICE
    pieces = quarter // slice_rows
    my_group = lax.axis_index("gx")
    my_lane = lax.axis_index("gy")
    n_gy = lax.axis_size("gy")
    first = my_group * owned
    waves = fetch_list.shape[0]
    pair_p = [(lane, lane ^ 1) for lane in range(n_gy)]
    pair_r = [(lane, n_gy - 1 - lane) for lane in range(n_gy)]
    lane_p = jnp.bitwise_xor(my_lane, 1)
    lane_r = n_gy - 1 - my_lane
    own_unit = normalize(embeds)
    other_unit = lax.ppermute(own_unit, "gy", pair_p)
    own_pieces = own_unit.reshape(owned, pieces, slice_rows, width)
    own_counts = lax.dynamic_slice_in_dim(counts, first, owned)
    positions = jnp.arange(quarter, dtype=jnp.int32)
    col_sources = []
    for lane, unit in ((my_lane, own_unit), (lane_p, other_unit)):
        col_limit = (own_counts - lane * quarter).astype(jnp.int32)
        col_sources.append((unit, col_limit))
    slice_offsets = jnp.arange(slice_rows, dtype=jnp.int32)
    local_ids = jnp.arange(owned, dtype=jnp.int32)
    piece_ids = jnp.arange(pieces, dtype=jnp.int32)
    col_part = [jnp.full((owned, quarter), -1.0, jnp.float32) for _ in col_sources]
    sent_blocks = []
    sent_pieces = []
    jobs = []
    for wave_index in range(waves):
        tiles = lax.dynamic_index_in_dim(fetch_list[wave_index], my_group, 1, False)
        outgoing_sent_block = tiles // pieces - first
        outgoing_sent_piece = tiles % pieces
        sent_blocks.append(outgoing_sent_block)
        sent_pieces.append(outgoing_sent_piece)
        outbound = own_pieces[outgoing_sent_block, outgoing_sent_piece]
        arrived = lax.all_to_all(outbound, "gx", split_axis=0, concat_axis=0, tiled=True)
        arrived_other = lax.ppermute(arrived, "gy", pair_r)
        incoming = lax.dynamic_index_in_dim(fetch_list[wave_index], my_group, 0, False)
        arrived_counts = counts[incoming // pieces]
        chosen = lax.dynamic_index_in_dim(partners[wave_index], my_group, 0, False) - first
        listed = jnp.any(chosen[:, :, None] == local_ids[None, None, :], axis=1)
        piece_rows = (incoming % pieces)[:, None] * slice_rows + slice_offsets[None, :]
        for part, (lane, rows_in) in enumerate(((my_lane, arrived), (lane_r, arrived_other))):
            row_valid = (lane * quarter + piece_rows) < arrived_counts[:, None]
            jobs.append((wave_index, part, rows_in, row_valid, listed))
    row_best = {}
    token = None
    order = sorted(
        ((source, job) for source in range(len(col_sources)) for job in range(len(jobs))),
        key=lambda item: (jobs[item[1]][0] == waves - 1 and jobs[item[1]][1] == 1, item[0], item[1]),
    )
    for source, job in order:
        unit, col_limit = col_sources[source]
        wave_index, part, rows_in, row_valid, listed = jobs[job]
        if token is not None:
            token, rows_in, unit = lax.optimization_barrier((token, rows_in, unit))
        rows_max, col_best = lent_scores(rows_in, row_valid, listed, unit, col_limit)
        token = (rows_max, col_best)
        key = (wave_index, part)
        row_best[key] = rows_max if key not in row_best else jnp.maximum(row_best[key], rows_max)
        col_part[source] = jnp.maximum(col_part[source], col_best)
    row_mine_parts = [row_best[(wave_index, 0)] for wave_index in range(waves)]
    row_other_parts = [row_best[(wave_index, 1)] for wave_index in range(waves)]
    col_back = lax.ppermute(col_part[1], "gy", pair_p)
    col_total = jnp.maximum(col_part[0], col_back)
    row_other = jnp.stack(row_other_parts, axis=0)
    row_back = lax.ppermute(row_other, "gy", pair_r)
    row_mine = jnp.maximum(jnp.stack(row_mine_parts, axis=0), row_back)
    returned = lax.all_to_all(row_mine, "gx", split_axis=1, concat_axis=1, tiled=True)
    row_total = jnp.full((owned, pieces, slice_rows), -1.0, jnp.float32)
    for wave_index in range(waves):
        match = (sent_blocks[wave_index][:, None, None] == local_ids[None, :, None]) & (
            sent_pieces[wave_index][:, None, None] == piece_ids[None, None, :]
        )
        placed = jnp.max(
            jnp.where(
                match[:, :, :, None], returned[wave_index][:, None, None, :], jnp.float32(-1.0)
            ),
            axis=0,
        )
        row_total = jnp.maximum(row_total, placed)
    nearest = jnp.maximum(row_total.reshape(owned, quarter), col_total)
    mine_valid = (my_lane * quarter + positions)[None, :] < own_counts[:, None]
    return jnp.where(mine_valid, nearest, jnp.float32(-1.0))


def solution(mesh):
    in_specs = (P("gx", "gy", None), P(), P(), P())
    out_specs = P("gx", "gy")
    return jax.shard_map(
        device_body, mesh=mesh, in_specs=in_specs, out_specs=out_specs, check_vma=False
    )
```

```python
import jax
import jax.numpy as jnp
from jax import lax
from jax.sharding import PartitionSpec as P


SLICE = 8


EPS = 1e-06


def normalize(source):
    values = source.astype(jnp.float32)
    return (values * lax.rsqrt(jnp.sum(values * values, axis=-1, keepdims=True) + EPS)).astype(
        jnp.bfloat16
    )


def lent_scores(lent, row_valid, listed, columns, col_limit):
    slots, lent_rows, width = lent.shape
    owned, quarter, _ = columns.shape
    flat_rows = lent.reshape(slots * lent_rows, width)
    scores = jnp.einsum("rd,kcd->rkc", flat_rows, columns, preferred_element_type=jnp.float32)
    scores = scores.reshape(slots, lent_rows, owned, quarter)
    col_valid = jnp.arange(quarter, dtype=jnp.int32)[None, :] < col_limit[:, None]
    keep = row_valid[:, :, None, None] & listed[:, None, :, None] & col_valid[None, None, :, :]
    scores = jnp.where(keep, scores, jnp.float32(-1.0))
    return jnp.max(scores, axis=(2, 3)), jnp.max(scores, axis=(0, 1))


def device_body(embeds, fetch_list, partners, counts):
    owned, quarter, width = embeds.shape
    slice_rows = SLICE
    pieces = quarter // slice_rows
    my_group = lax.axis_index("gx")
    my_lane = lax.axis_index("gy")
    n_gy = lax.axis_size("gy")
    first = my_group * owned
    waves = fetch_list.shape[0]
    pair_p = [(lane, lane ^ 1) for lane in range(n_gy)]
    pair_r = [(lane, n_gy - 1 - lane) for lane in range(n_gy)]
    lane_p = jnp.bitwise_xor(my_lane, 1)
    lane_r = n_gy - 1 - my_lane
    own_unit = normalize(embeds)
    other_unit = lax.ppermute(own_unit, "gy", pair_p)
    own_pieces = own_unit.reshape(owned, pieces, slice_rows, width)
    own_counts = lax.dynamic_slice_in_dim(counts, first, owned)
    positions = jnp.arange(quarter, dtype=jnp.int32)
    col_sources = []
    for lane, unit in ((my_lane, own_unit), (lane_p, other_unit)):
        col_limit = (own_counts - lane * quarter).astype(jnp.int32)
        col_sources.append((unit, col_limit))
    slice_offsets = jnp.arange(slice_rows, dtype=jnp.int32)
    local_ids = jnp.arange(owned, dtype=jnp.int32)
    piece_ids = jnp.arange(pieces, dtype=jnp.int32)
    col_part = [jnp.full((owned, quarter), -1.0, jnp.float32) for _ in col_sources]
    sent_blocks = []
    sent_pieces = []
    jobs = []
    for wave_index in range(waves):
        tiles = lax.dynamic_index_in_dim(fetch_list[wave_index], my_group, 1, False)
        outgoing_sent_block = tiles // pieces - first
        outgoing_sent_piece = tiles % pieces
        sent_blocks.append(outgoing_sent_block)
        sent_pieces.append(outgoing_sent_piece)
        outbound = own_pieces[outgoing_sent_block, outgoing_sent_piece]
        arrived = lax.all_to_all(outbound, "gx", split_axis=0, concat_axis=0, tiled=True)
        halves = 2 if wave_index == waves - 1 else 1
        span = arrived.shape[0] // halves
        arrived_other = []
        for half in range(halves):
            piece = arrived[half * span : (half + 1) * span]
            arrived_other.append(lax.ppermute(piece, "gy", pair_r))
        incoming = lax.dynamic_index_in_dim(fetch_list[wave_index], my_group, 0, False)
        arrived_counts = counts[incoming // pieces]
        chosen = lax.dynamic_index_in_dim(partners[wave_index], my_group, 0, False) - first
        listed = jnp.any(chosen[:, :, None] == local_ids[None, None, :], axis=1)
        piece_rows = (incoming % pieces)[:, None] * slice_rows + slice_offsets[None, :]
        row_valid = (my_lane * quarter + piece_rows) < arrived_counts[:, None]
        jobs.append((wave_index, 0, 0, arrived, row_valid, listed))
        row_valid = (lane_r * quarter + piece_rows) < arrived_counts[:, None]
        for half, rows_in in enumerate(arrived_other):
            cut = slice(half * span, (half + 1) * span)
            jobs.append((wave_index, 1, half, rows_in, row_valid[cut], listed[cut]))
    row_best = {}
    token = None
    order = sorted(
        ((source, job) for source in range(len(col_sources)) for job in range(len(jobs))),
        key=lambda item: (
            jobs[item[1]][0] == waves - 1 and jobs[item[1]][1] == 1,
            jobs[item[1]][2],
            item[0],
            item[1],
        ),
    )
    for source, job in order:
        unit, col_limit = col_sources[source]
        wave_index, part, half, rows_in, row_valid, listed = jobs[job]
        if token is not None:
            token, rows_in, unit = lax.optimization_barrier((token, rows_in, unit))
        rows_max, col_best = lent_scores(rows_in, row_valid, listed, unit, col_limit)
        token = (rows_max, col_best)
        key = (wave_index, part, half)
        row_best[key] = rows_max if key not in row_best else jnp.maximum(row_best[key], rows_max)
        col_part[source] = jnp.maximum(col_part[source], col_best)
    row_mine_parts = [row_best[(wave_index, 0, 0)] for wave_index in range(waves)]
    row_other_parts = []
    for wave_index in range(waves):
        pieces_of = sorted(k for k in row_best if k[0] == wave_index and k[1] == 1)
        row_other_parts.append(jnp.concatenate([row_best[k] for k in pieces_of], axis=0))
    col_back = lax.ppermute(col_part[1], "gy", pair_p)
    col_total = jnp.maximum(col_part[0], col_back)
    row_other = jnp.stack(row_other_parts, axis=0)
    row_back = lax.ppermute(row_other, "gy", pair_r)
    row_mine = jnp.maximum(jnp.stack(row_mine_parts, axis=0), row_back)
    returned = lax.all_to_all(row_mine, "gx", split_axis=1, concat_axis=1, tiled=True)
    row_total = jnp.full((owned, pieces, slice_rows), -1.0, jnp.float32)
    for wave_index in range(waves):
        match = (sent_blocks[wave_index][:, None, None] == local_ids[None, :, None]) & (
            sent_pieces[wave_index][:, None, None] == piece_ids[None, None, :]
        )
        placed = jnp.max(
            jnp.where(
                match[:, :, :, None], returned[wave_index][:, None, None, :], jnp.float32(-1.0)
            ),
            axis=0,
        )
        row_total = jnp.maximum(row_total, placed)
    nearest = jnp.maximum(row_total.reshape(owned, quarter), col_total)
    mine_valid = (my_lane * quarter + positions)[None, :] < own_counts[:, None]
    return jnp.where(mine_valid, nearest, jnp.float32(-1.0))


def solution(mesh):
    in_specs = (P("gx", "gy", None), P(), P(), P())
    out_specs = P("gx", "gy")
    return jax.shard_map(
        device_body, mesh=mesh, in_specs=in_specs, out_specs=out_specs, check_vma=False
    )
```

```python
import jax
import jax.numpy as jnp
from jax import lax
from jax.experimental import pallas as pl
from jax.experimental.pallas import tpu as pltpu
from jax.sharding import PartitionSpec as P


SLICE = 8


EPS = 1e-06


def normalize(source):
    values = source.astype(jnp.float32)
    return (values * lax.rsqrt(jnp.sum(values * values, axis=-1, keepdims=True) + EPS)).astype(
        jnp.bfloat16
    )


def _stage_kernel(source_ref, staged_ref):
    pltpu.sync_copy(source_ref, staged_ref)


def stage_in_vmem(source):
    return pl.pallas_call(
        _stage_kernel,
        out_shape=jax.ShapeDtypeStruct(source.shape, source.dtype),
        in_specs=[pl.BlockSpec(memory_space=pl.ANY)],
        out_specs=pl.BlockSpec(memory_space=pltpu.VMEM),
        cost_estimate=pl.CostEstimate(flops=0, transcendentals=0, bytes_accessed=2 * source.nbytes),
    )(source)


def lent_scores(lent, row_valid, listed, columns, col_limit):
    slots, lent_rows, width = lent.shape
    owned, quarter, _ = columns.shape
    flat_rows = lent.reshape(slots * lent_rows, width)
    scores = jnp.einsum("rd,kcd->rkc", flat_rows, columns, preferred_element_type=jnp.float32)
    scores = scores.reshape(slots, lent_rows, owned, quarter)
    col_valid = jnp.arange(quarter, dtype=jnp.int32)[None, :] < col_limit[:, None]
    keep = row_valid[:, :, None, None] & listed[:, None, :, None] & col_valid[None, None, :, :]
    scores = jnp.where(keep, scores, jnp.float32(-1.0))
    return jnp.max(scores, axis=(2, 3)), jnp.max(scores, axis=(0, 1))


def device_body(embeds, fetch_list, partners, counts):
    owned, quarter, width = embeds.shape
    slice_rows = SLICE
    pieces = quarter // slice_rows
    my_group = lax.axis_index("gx")
    my_lane = lax.axis_index("gy")
    n_gy = lax.axis_size("gy")
    first = my_group * owned
    waves = fetch_list.shape[0]
    pair_p = [(lane, lane ^ 1) for lane in range(n_gy)]
    pair_r = [(lane, n_gy - 1 - lane) for lane in range(n_gy)]
    lane_p = jnp.bitwise_xor(my_lane, 1)
    lane_r = n_gy - 1 - my_lane
    own_unit = normalize(embeds)
    other_unit = lax.ppermute(own_unit, "gy", pair_p)
    own_pieces = own_unit.reshape(owned, pieces, slice_rows, width)
    own_counts = lax.dynamic_slice_in_dim(counts, first, owned)
    positions = jnp.arange(quarter, dtype=jnp.int32)
    col_sources = []
    for lane, unit in ((my_lane, stage_in_vmem(own_unit)), (lane_p, stage_in_vmem(other_unit))):
        col_limit = (own_counts - lane * quarter).astype(jnp.int32)
        col_sources.append((unit, col_limit))
    slice_offsets = jnp.arange(slice_rows, dtype=jnp.int32)
    local_ids = jnp.arange(owned, dtype=jnp.int32)
    piece_ids = jnp.arange(pieces, dtype=jnp.int32)
    col_part = [jnp.full((owned, quarter), -1.0, jnp.float32) for _ in col_sources]
    sent_blocks = []
    sent_pieces = []
    jobs = []
    for wave_index in range(waves):
        tiles = lax.dynamic_index_in_dim(fetch_list[wave_index], my_group, 1, False)
        outgoing_sent_block = tiles // pieces - first
        outgoing_sent_piece = tiles % pieces
        sent_blocks.append(outgoing_sent_block)
        sent_pieces.append(outgoing_sent_piece)
        outbound = own_pieces[outgoing_sent_block, outgoing_sent_piece]
        arrived = lax.all_to_all(outbound, "gx", split_axis=0, concat_axis=0, tiled=True)
        arrived_other = lax.ppermute(arrived, "gy", pair_r)
        incoming = lax.dynamic_index_in_dim(fetch_list[wave_index], my_group, 0, False)
        arrived_counts = counts[incoming // pieces]
        chosen = lax.dynamic_index_in_dim(partners[wave_index], my_group, 0, False) - first
        listed = jnp.any(chosen[:, :, None] == local_ids[None, None, :], axis=1)
        piece_rows = (incoming % pieces)[:, None] * slice_rows + slice_offsets[None, :]
        for part, (lane, rows_in) in enumerate(((my_lane, arrived), (lane_r, arrived_other))):
            row_valid = (lane * quarter + piece_rows) < arrived_counts[:, None]
            jobs.append((wave_index, part, rows_in, row_valid, listed))
    row_best = {}
    token = None
    order = sorted(
        ((source, job) for source in range(len(col_sources)) for job in range(len(jobs))),
        key=lambda item: (jobs[item[1]][0] == waves - 1 and jobs[item[1]][1] == 1, item[0], item[1]),
    )
    for source, job in order:
        unit, col_limit = col_sources[source]
        wave_index, part, rows_in, row_valid, listed = jobs[job]
        if token is not None:
            token, rows_in, unit = lax.optimization_barrier((token, rows_in, unit))
        rows_max, col_best = lent_scores(rows_in, row_valid, listed, unit, col_limit)
        token = (rows_max, col_best)
        key = (wave_index, part)
        row_best[key] = rows_max if key not in row_best else jnp.maximum(row_best[key], rows_max)
        col_part[source] = jnp.maximum(col_part[source], col_best)
    row_mine_parts = [row_best[(wave_index, 0)] for wave_index in range(waves)]
    row_other_parts = [row_best[(wave_index, 1)] for wave_index in range(waves)]
    col_back = lax.ppermute(col_part[1], "gy", pair_p)
    col_total = jnp.maximum(col_part[0], col_back)
    row_other = jnp.stack(row_other_parts, axis=0)
    row_back = lax.ppermute(row_other, "gy", pair_r)
    row_mine = jnp.maximum(jnp.stack(row_mine_parts, axis=0), row_back)
    returned = lax.all_to_all(row_mine, "gx", split_axis=1, concat_axis=1, tiled=True)
    row_total = jnp.full((owned, pieces, slice_rows), -1.0, jnp.float32)
    for wave_index in range(waves):
        match = (sent_blocks[wave_index][:, None, None] == local_ids[None, :, None]) & (
            sent_pieces[wave_index][:, None, None] == piece_ids[None, None, :]
        )
        placed = jnp.max(
            jnp.where(
                match[:, :, :, None], returned[wave_index][:, None, None, :], jnp.float32(-1.0)
            ),
            axis=0,
        )
        row_total = jnp.maximum(row_total, placed)
    nearest = jnp.maximum(row_total.reshape(owned, quarter), col_total)
    mine_valid = (my_lane * quarter + positions)[None, :] < own_counts[:, None]
    return jnp.where(mine_valid, nearest, jnp.float32(-1.0))


def solution(mesh):
    in_specs = (P("gx", "gy", None), P(), P(), P())
    out_specs = P("gx", "gy")
    return jax.shard_map(
        device_body, mesh=mesh, in_specs=in_specs, out_specs=out_specs, check_vma=False
    )
```
